32 devices in a mesh: grad: 4 (over y, x), col: 8 (over z, core).
Axes of the slice: x: 2, y: 2, z: 4, core: 2. Of those that a mesh axis runs over, the one named last changes fastest.
Arguments:
- gradient: bfloat16 [16384, 53248], P(('grad', 'col'))
- test_matrix: bfloat16 [16384, 256], P(('grad', 'col')), may hold values from -6 to 6
Outputs:
- low_rank: float32 [16384, 256], P(('grad', 'col'))
- projector: float32 [53248, 256], P('col')
The draws below stay inside these ranges and needn't reach their ends.
All inputs are finite; a program needn't handle non-finite values.
Results may differ from the reference program's by a relative error of at most 0.008.
Values may be sent and summed in bfloat16 or wider, within the bound.
No kernel may reach another device: no remote copies, remote signals or barrier semaphores. Data moves between devices by JAX's collectives and lax.ppermute only.
A program may use at most 256 MiB of HBM per device.

```python
import math
import jax
import jax.numpy as jnp
from jax import lax

D = 16384
FF = 53248
RANK = 256
POWER = 2


def draw_gradient(key, part):
    noise_key = jax.random.fold_in(key, 11)
    column_key = jax.random.fold_in(key, 12)
    row_key = jax.random.fold_in(key, 13)
    position = jnp.arange(FF, dtype=jnp.float32) / (FF - 1)
    rough = jnp.exp(jax.random.uniform(column_key, (FF,), jnp.float32, 0.0, math.log(3.0)))
    row_scale = jnp.exp(jax.random.uniform(row_key, (D, 1), jnp.float32, 0.0, math.log(3.0)))
    rising = jnp.exp(math.log(6.0) * position)
    noise = jax.random.normal(noise_key, (D, FF), jnp.float32)
    scaled = noise * row_scale * (rising * rough)[None, :] / (4.0 * math.sqrt(FF))
    return scaled.astype(jnp.bfloat16)


def level_of(stream_key, shape, shards, least, largest):
    def one(dim, blocks):
        steps = jax.random.uniform(jax.random.fold_in(jax.random.fold_in(stream_key, 6), dim), (blocks,), jnp.float32, least / len(shards), largest / len(shards))
        return jnp.repeat(jnp.exp(steps), shape[dim] // blocks).reshape((-1,) + (1,) * (len(shape) - dim - 1))

    factor_of = one(*shards[0])
    for cut in shards[1:]:
        factor_of = factor_of * one(*cut)
    return factor_of


def gaussian(own_key, dims, deviation, bound, split=(), kind=jnp.bfloat16):
    level = level_of(own_key, dims, split, -0.22, 0.18) if split else 1.0
    array = jax.random.normal(own_key, dims, jnp.float32) * deviation * level
    return jnp.minimum(jnp.maximum(array, -bound), bound).astype(kind)


def setup_inputs(seed: int = 0) -> dict:
    splits = jax.random.split(jax.random.key(seed), 3)
    gradient = draw_gradient(jax.random.fold_in(splits[2], 71), 0)
    test_matrix = gaussian(splits[1], (D, RANK), 1.0, 6.0, ((0, 32),))
    return dict(gradient=gradient, test_matrix=test_matrix)


def orthonormal(matrix):
    gram = lax.dot_general(matrix.astype(jnp.float32), matrix.astype(jnp.float32), (((0,), (0,)), ((), ())), precision=lax.Precision.HIGHEST, preferred_element_type=jnp.float32)
    lower_factor = jnp.linalg.cholesky(gram)
    return lax.linalg.triangular_solve(lower_factor, matrix, left_side=False, lower=True, transpose_a=True)

def reference(gradient, test_matrix):
    sketch = lax.dot_general(gradient.astype(jnp.float32), test_matrix.astype(jnp.float32), (((0,), (0,)), ((), ())), preferred_element_type=jnp.float32)
    for iteration in range(POWER + 1):
        basis_block = orthonormal(sketch)
        reduced = jnp.dot(gradient.astype(jnp.float32), basis_block.astype(jnp.bfloat16).astype(jnp.float32), preferred_element_type=jnp.float32)
        if iteration < POWER:
            sketch = lax.dot_general(gradient.astype(jnp.float32), reduced.astype(jnp.bfloat16).astype(jnp.float32), (((0,), (0,)), ((), ())), preferred_element_type=jnp.float32)
    return (reduced, basis_block * math.sqrt(FF))
```

```python
import math

import jax
import jax.numpy as jnp
from jax import lax
from jax.sharding import PartitionSpec as P

FF = 53248
POWER = 2


def orthonormal(rows):
    partial_gram = lax.dot_general(
        rows,
        rows,
        (((0,), (0,)), ((), ())),
        precision=lax.Precision.HIGHEST,
        preferred_element_type=jnp.float32,
    )
    gram = lax.psum(partial_gram, ("grad", "col"))
    lower_factor = jnp.linalg.cholesky(gram)
    return lax.linalg.triangular_solve(
        lower_factor, rows, left_side=False, lower=True, transpose_a=True
    )


def shards(gradient, test_matrix):
    n_grad = lax.axis_size("grad")
    n_col = lax.axis_size("col")
    n_rows, n_ff = gradient.shape
    piece = n_ff // (n_col * n_grad)
    split = gradient.reshape(n_rows, n_col, n_grad, piece)
    blocks = lax.all_to_all(split, "grad", split_axis=2, concat_axis=0, tiled=True)
    blocks = blocks.reshape(n_grad * n_rows, n_col * piece)

    def sketch_of(row_piece):
        rows = lax.all_gather(row_piece, "grad", axis=0, tiled=True)
        partial = lax.dot_general(
            blocks, rows, (((0,), (0,)), ((), ())), preferred_element_type=jnp.float32
        )
        return lax.psum_scatter(partial, "col", scatter_dimension=0, tiled=True)

    sketch = sketch_of(test_matrix)
    for iteration in range(POWER + 1):
        basis_rows = orthonormal(sketch)
        basis_bf = lax.all_gather(basis_rows.astype(jnp.bfloat16), "col", axis=0, tiled=True)
        reduced = lax.psum_scatter(
            jnp.dot(blocks, basis_bf, preferred_element_type=jnp.float32),
            "grad",
            scatter_dimension=0,
            tiled=True,
        )
        if iteration < POWER:
            sketch = sketch_of(reduced.astype(jnp.bfloat16))
    projector = lax.all_gather(basis_rows * math.sqrt(FF), "grad", axis=0, tiled=True)
    return (reduced, projector)


def solution(mesh):
    return jax.shard_map(
        shards,
        mesh=mesh,
        in_specs=(P(("grad", "col"), None), P(("grad", "col"), None)),
        out_specs=(P(("grad", "col"), None), P("col", None)),
        check_vma=False,
    )
```

```python
import math

import jax
import jax.numpy as jnp
from jax import lax
from jax.sharding import PartitionSpec as P

FF = 53248
POWER = 2
HALVES = 2


def all_sum(value, axes):
    for axis in axes:
        size = lax.axis_size(axis)
        if size & (size - 1):
            value = lax.psum(value, axis)
            continue
        step = 1
        while step < size:
            value = value + lax.ppermute(value, axis, [(i, i ^ step) for i in range(size)])
            step *= 2
    return value


def orthonormal(rows):
    partial_gram = lax.dot_general(
        rows,
        rows,
        (((0,), (0,)), ((), ())),
        precision=lax.Precision.HIGHEST,
        preferred_element_type=jnp.float32,
    )
    gram = all_sum(partial_gram, ("col", "grad"))
    lower_factor = jnp.linalg.cholesky(gram)
    return lax.linalg.triangular_solve(
        lower_factor, rows, left_side=False, lower=True, transpose_a=True
    )


def shards(gradient, test_matrix):
    n_grad = lax.axis_size("grad")
    n_col = lax.axis_size("col")
    n_rows, n_ff = gradient.shape
    piece = n_ff // (n_col * n_grad)
    half = piece // HALVES
    split = gradient.reshape(n_rows, n_col, n_grad, HALVES, half)
    chunks = []
    for h in range(HALVES):
        moved = lax.all_to_all(split[:, :, :, h], "grad", split_axis=2, concat_axis=0, tiled=True)
        chunks.append(moved.reshape(n_grad * n_rows, n_col * half))

    def sketch_of(row_piece):
        rows = lax.all_gather(row_piece, "grad", axis=0, tiled=True)
        parts = []
        for chunk in chunks:
            partial = lax.dot_general(
                chunk, rows, (((0,), (0,)), ((), ())), preferred_element_type=jnp.float32
            )
            parts.append(lax.psum_scatter(partial, "col", scatter_dimension=0, tiled=True))
        return jnp.concatenate(parts, axis=0)

    sketch = sketch_of(test_matrix)
    for iteration in range(POWER + 1):
        basis_rows = orthonormal(sketch)
        basis_bf = lax.all_gather(
            basis_rows.astype(jnp.bfloat16).reshape(HALVES, half, -1), "col", axis=1, tiled=True
        )
        partial = jnp.dot(chunks[0], basis_bf[0], preferred_element_type=jnp.float32)
        for h in range(1, HALVES):
            partial = partial + jnp.dot(chunks[h], basis_bf[h], preferred_element_type=jnp.float32)
        reduced = lax.psum_scatter(partial, "grad", scatter_dimension=0, tiled=True)
        if iteration < POWER:
            sketch = sketch_of(reduced.astype(jnp.bfloat16))
    projector = lax.all_gather(basis_rows * math.sqrt(FF), "grad", axis=0, tiled=True)
    return (reduced, projector)


def solution(mesh):
    return jax.shard_map(
        shards,
        mesh=mesh,
        in_specs=(P(("grad", "col"), None), P(("grad", "col"), None)),
        out_specs=(P(("grad", "col"), None), P("col", None)),
        check_vma=False,
    )
```

```python
import math

import jax
import jax.numpy as jnp
from jax import lax
from jax.experimental.layout import Layout, with_layout_constraint
from jax.sharding import Mesh, PartitionSpec as P

FF = 53248
POWER = 2
HALVES = 2
COL = ("chip", "core")


def all_sum(value, axes):
    for axis in axes:
        size = lax.axis_size(axis)
        if size & (size - 1):
            value = lax.psum(value, axis)
            continue
        step = 1
        while step < size:
            value = value + lax.ppermute(value, axis, [(i, i ^ step) for i in range(size)])
            step *= 2
    return value


def orthonormal(rows):
    partial_gram = lax.dot_general(
        rows,
        rows,
        (((0,), (0,)), ((), ())),
        precision=lax.Precision.HIGHEST,
        preferred_element_type=jnp.float32,
    )
    gram = all_sum(partial_gram, ("core", "chip", "grad"))
    lower_factor = jnp.linalg.cholesky(gram)
    return lax.linalg.triangular_solve(
        lower_factor, rows, left_side=False, lower=True, transpose_a=True
    )


def shards(gradient, test_matrix):
    n_grad = lax.axis_size("grad")
    n_chip = lax.axis_size("chip")
    n_col = n_chip * lax.axis_size("core")
    n_rows, n_ff = gradient.shape
    piece = n_ff // (n_col * n_grad)
    half = piece // HALVES
    split = gradient.reshape(n_rows, n_col, n_grad, HALVES, half)
    chunks = []
    for h in range(HALVES):
        moved = lax.all_to_all(split[:, :, :, h], "grad", split_axis=2, concat_axis=0, tiled=True)
        chunk = moved.reshape(n_grad * n_rows, n_col * half)
        chunks.append(with_layout_constraint(chunk, Layout((0, 1))))

    def sketch_of(row_piece):
        rows = lax.all_gather(row_piece, "grad", axis=0, tiled=True)
        parts = []
        for chunk in chunks:
            partial = lax.dot_general(
                chunk, rows, (((0,), (0,)), ((), ())), preferred_element_type=jnp.float32
            )
            parts.append(lax.psum_scatter(partial, COL, scatter_dimension=0, tiled=True))
        return jnp.concatenate(parts, axis=0)

    sketch = sketch_of(test_matrix)
    for iteration in range(POWER + 1):
        basis_rows = orthonormal(sketch)
        basis_bf = lax.all_gather(
            basis_rows.astype(jnp.bfloat16).reshape(HALVES, 1, half, -1), "chip", axis=1, tiled=True
        )
        basis_bf = lax.all_gather(basis_bf, "core", axis=1)
        basis_bf = jnp.swapaxes(basis_bf, 1, 2).reshape(HALVES, n_col * half, -1)
        partial = jnp.dot(chunks[0], basis_bf[0], preferred_element_type=jnp.float32)
        for h in range(1, HALVES):
            partial = partial + jnp.dot(chunks[h], basis_bf[h], preferred_element_type=jnp.float32)
        reduced = lax.psum_scatter(partial, "grad", scatter_dimension=0, tiled=True)
        if iteration < POWER:
            sketch = sketch_of(reduced.astype(jnp.bfloat16))
    projector = lax.all_gather(basis_rows * math.sqrt(FF), "grad", axis=0, tiled=True)
    return (reduced, projector)


def solution(mesh):
    n_grad, n_col = mesh.devices.shape
    split_mesh = Mesh(mesh.devices.reshape(n_grad, n_col // 2, 2), ("grad",) + COL)
    return jax.shard_map(
        shards,
        mesh=split_mesh,
        in_specs=(P(("grad",) + COL, None), P(("grad",) + COL, None)),
        out_specs=(P(("grad",) + COL, None), P(COL, None)),
        check_vma=False,
    )
```

```python
import math

import jax
import jax.numpy as jnp
from jax import lax
from jax.sharding import PartitionSpec as P

FF = 53248
POWER = 2
HALVES = 2


def all_sum(value, axes):
    for axis in axes:
        size = lax.axis_size(axis)
        if size & (size - 1):
            value = lax.psum(value, axis)
            continue
        step = 1
        while step < size:
            value = value + lax.ppermute(value, axis, [(i, i ^ step) for i in range(size)])
            step *= 2
    return value


def grad_gather(value):
    size = lax.axis_size("grad")
    index = lax.axis_index("grad")
    received = [value] + [
        lax.ppermute(value, "grad", [(i, (i + s) % size) for i in range(size)])
        for s in range(1, size)
    ]
    ordered = jnp.roll(jnp.stack(received)[::-1], index + 1, axis=0)
    return ordered.reshape((size * value.shape[0],) + value.shape[1:])


def grad_scatter_sum(value):
    size = lax.axis_size("grad")
    index = lax.axis_index("grad")
    pieces = value.reshape((size, value.shape[0] // size) + value.shape[1:])
    total = lax.dynamic_index_in_dim(pieces, index, keepdims=False)
    for s in range(1, size):
        outgoing = lax.dynamic_index_in_dim(pieces, (index + s) % size, keepdims=False)
        total = total + lax.ppermute(outgoing, "grad", [(i, (i + s) % size) for i in range(size)])
    return total


def orthonormal(rows):
    partial_gram = lax.dot_general(
        rows,
        rows,
        (((0,), (0,)), ((), ())),
        precision=lax.Precision.HIGHEST,
        preferred_element_type=jnp.float32,
    )
    gram = all_sum(partial_gram, ("col", "grad"))
    lower_factor = jnp.linalg.cholesky(gram)
    return lax.linalg.triangular_solve(
        lower_factor, rows, left_side=False, lower=True, transpose_a=True
    )


def shards(gradient, test_matrix):
    n_grad = lax.axis_size("grad")
    n_col = lax.axis_size("col")
    n_rows, n_ff = gradient.shape
    piece = n_ff // (n_col * n_grad)
    half = piece // HALVES
    split = gradient.reshape(n_rows, n_col, n_grad, HALVES, half)
    chunks = []
    for h in range(HALVES):
        moved = lax.all_to_all(split[:, :, :, h], "grad", split_axis=2, concat_axis=0, tiled=True)
        chunks.append(moved.reshape(n_grad * n_rows, n_col * half))

    def sketch_of(row_piece):
        rows = grad_gather(row_piece)
        parts = []
        for chunk in chunks:
            partial = lax.dot_general(
                chunk, rows, (((0,), (0,)), ((), ())), preferred_element_type=jnp.float32
            )
            parts.append(lax.psum_scatter(partial, "col", scatter_dimension=0, tiled=True))
        return jnp.concatenate(parts, axis=0)

    sketch = sketch_of(test_matrix)
    for iteration in range(POWER + 1):
        basis_rows = orthonormal(sketch)
        basis_bf = lax.all_gather(
            basis_rows.astype(jnp.bfloat16).reshape(HALVES, half, -1), "col", axis=1, tiled=True
        )
        partial = jnp.dot(chunks[0], basis_bf[0], preferred_element_type=jnp.float32)
        for h in range(1, HALVES):
            partial = partial + jnp.dot(chunks[h], basis_bf[h], preferred_element_type=jnp.float32)
        reduced = grad_scatter_sum(partial)
        if iteration < POWER:
            sketch = sketch_of(reduced.astype(jnp.bfloat16))
    projector = grad_gather(basis_rows * math.sqrt(FF))
    return (reduced, projector)


def solution(mesh):
    return jax.shard_map(
        shards,
        mesh=mesh,
        in_specs=(P(("grad", "col"), None), P(("grad", "col"), None)),
        out_specs=(P(("grad", "col"), None), P("col", None)),
        check_vma=False,
    )
```

```python
import math

import jax
import jax.numpy as jnp
from jax import lax
from jax.sharding import PartitionSpec as P

FF = 53248
POWER = 2
HALVES = 2


def all_sum(value, axes):
    for axis in axes:
        size = lax.axis_size(axis)
        if size & (size - 1):
            value = lax.psum(value, axis)
            continue
        step = 1
        while step < size:
            value = value + lax.ppermute(value, axis, [(i, i ^ step) for i in range(size)])
            step *= 2
    return value


def grad_gather(value):
    size = lax.axis_size("grad")
    index = lax.axis_index("grad")
    received = [value] + [
        lax.ppermute(value, "grad", [(i, (i + s) % size) for i in range(size)])
        for s in range(1, size)
    ]
    ordered = jnp.roll(jnp.stack(received)[::-1], index + 1, axis=0)
    return ordered.reshape((size * value.shape[0],) + value.shape[1:])


def grad_scatter_sum(value):
    size = lax.axis_size("grad")
    index = lax.axis_index("grad")
    pieces = value.reshape((size, value.shape[0] // size) + value.shape[1:])
    total = lax.dynamic_index_in_dim(pieces, index, keepdims=False)
    for s in range(1, size):
        outgoing = lax.dynamic_index_in_dim(pieces, (index + s) % size, keepdims=False)
        total = total + lax.ppermute(outgoing, "grad", [(i, (i + s) % size) for i in range(size)])
    return total


def orthonormal(rows):
    partial_gram = lax.dot_general(
        rows,
        rows,
        (((0,), (0,)), ((), ())),
        precision=lax.Precision.HIGHEST,
        preferred_element_type=jnp.float32,
    )
    gram = all_sum(partial_gram, ("col", "grad"))
    lower_factor = jnp.linalg.cholesky(gram)
    return lax.linalg.triangular_solve(
        lower_factor, rows, left_side=False, lower=True, transpose_a=True
    )


def shards(gradient, test_matrix):
    n_grad = lax.axis_size("grad")
    n_col = lax.axis_size("col")
    n_rows, n_ff = gradient.shape
    piece = n_ff // (n_col * n_grad)
    half = piece // HALVES
    test_rows, gradient = lax.optimization_barrier((grad_gather(test_matrix), gradient))
    split = gradient.reshape(n_rows, n_col, n_grad, HALVES, half)
    chunks = []
    for h in range(HALVES):
        moved = lax.all_to_all(split[:, :, :, h], "grad", split_axis=2, concat_axis=0, tiled=True)
        chunks.append(moved.reshape(n_grad * n_rows, n_col * half))

    def sketch_of(rows):
        parts = []
        for chunk in chunks:
            partial = lax.dot_general(
                chunk, rows, (((0,), (0,)), ((), ())), preferred_element_type=jnp.float32
            )
            parts.append(lax.psum_scatter(partial, "col", scatter_dimension=0, tiled=True))
        return jnp.concatenate(parts, axis=0)

    sketch = sketch_of(test_rows)
    for iteration in range(POWER + 1):
        basis_rows = orthonormal(sketch)
        basis_bf = lax.all_gather(
            basis_rows.astype(jnp.bfloat16).reshape(HALVES, half, -1), "col", axis=1, tiled=True
        )
        partial = jnp.dot(chunks[0], basis_bf[0], preferred_element_type=jnp.float32)
        for h in range(1, HALVES):
            partial = partial + jnp.dot(chunks[h], basis_bf[h], preferred_element_type=jnp.float32)
        reduced = grad_scatter_sum(partial)
        if iteration < POWER:
            sketch = sketch_of(grad_gather(reduced.astype(jnp.bfloat16)))
    projector = grad_gather(basis_rows * math.sqrt(FF))
    return (reduced, projector)


def solution(mesh):
    return jax.shard_map(
        shards,
        mesh=mesh,
        in_specs=(P(("grad", "col"), None), P(("grad", "col"), None)),
        out_specs=(P(("grad", "col"), None), P("col", None)),
        check_vma=False,
    )
```

```python
import math

import jax
import jax.numpy as jnp
from jax import lax
from jax.sharding import PartitionSpec as P

FF = 53248
POWER = 2
HALVES = 2


def all_sum(value, axes):
    for axis in axes:
        size = lax.axis_size(axis)
        if size & (size - 1):
            value = lax.psum(value, axis)
            continue
        step = 1
        while step < size:
            value = value + lax.ppermute(value, axis, [(i, i ^ step) for i in range(size)])
            step *= 2
    return value


def grad_gather(value):
    size = lax.axis_size("grad")
    index = lax.axis_index("grad")
    received = [value] + [
        lax.ppermute(value, "grad", [(i, (i + s) % size) for i in range(size)])
        for s in range(1, size)
    ]
    ordered = jnp.roll(jnp.stack(received)[::-1], index + 1, axis=0)
    return ordered.reshape((size * value.shape[0],) + value.shape[1:])


def shift_gather(value):
    size = lax.axis_size("grad")
    received = [value] + [
        lax.ppermute(value, "grad", [(i, (i + s) % size) for i in range(size)])
        for s in range(1, size)
    ]
    return jnp.concatenate(received, axis=0)


def shift_scatter_sum(value):
    size = lax.axis_size("grad")
    pieces = value.reshape((size, value.shape[0] // size) + value.shape[1:])
    total = pieces[0]
    for s in range(1, size):
        outgoing = pieces[(size - s) % size]
        total = total + lax.ppermute(outgoing, "grad", [(i, (i + s) % size) for i in range(size)])
    return total


def orthonormal(rows):
    partial_gram = lax.dot_general(
        rows,
        rows,
        (((0,), (0,)), ((), ())),
        precision=lax.Precision.HIGHEST,
        preferred_element_type=jnp.float32,
    )
    gram = all_sum(partial_gram, ("col", "grad"))
    lower_factor = jnp.linalg.cholesky(gram)
    return lax.linalg.triangular_solve(
        lower_factor, rows, left_side=False, lower=True, transpose_a=True
    )


def shards(gradient, test_matrix):
    n_grad = lax.axis_size("grad")
    n_col = lax.axis_size("col")
    n_rows, n_ff = gradient.shape
    piece = n_ff // (n_col * n_grad)
    half = piece // HALVES
    test_rows, gradient = lax.optimization_barrier((shift_gather(test_matrix), gradient))
    index = lax.axis_index("grad")
    split = gradient.reshape(n_rows, n_col, n_grad, HALVES, half)
    chunks = []
    for h in range(HALVES):
        part = split[:, :, :, h]
        received = [lax.dynamic_index_in_dim(part, index, axis=2, keepdims=False)]
        for s in range(1, n_grad):
            outgoing = lax.dynamic_index_in_dim(part, (index + s) % n_grad, axis=2, keepdims=False)
            received.append(
                lax.ppermute(outgoing, "grad", [(i, (i + s) % n_grad) for i in range(n_grad)])
            )
        moved = jnp.concatenate(received, axis=0)
        chunks.append(moved.reshape(n_grad * n_rows, n_col * half))

    def sketch_of(rows):
        parts = []
        for chunk in chunks:
            partial = lax.dot_general(
                chunk, rows, (((0,), (0,)), ((), ())), preferred_element_type=jnp.float32
            )
            parts.append(lax.psum_scatter(partial, "col", scatter_dimension=0, tiled=True))
        return jnp.concatenate(parts, axis=0)

    sketch = sketch_of(test_rows)
    for iteration in range(POWER + 1):
        basis_rows = orthonormal(sketch)
        basis_bf = lax.all_gather(
            basis_rows.astype(jnp.bfloat16).reshape(HALVES, half, -1), "col", axis=1, tiled=True
        )
        partial = jnp.dot(chunks[0], basis_bf[0], preferred_element_type=jnp.float32)
        for h in range(1, HALVES):
            partial = partial + jnp.dot(chunks[h], basis_bf[h], preferred_element_type=jnp.float32)
        reduced = shift_scatter_sum(partial)
        if iteration < POWER:
            sketch = sketch_of(shift_gather(reduced.astype(jnp.bfloat16)))
    projector = grad_gather(basis_rows * math.sqrt(FF))
    return (reduced, projector)


def solution(mesh):
    return jax.shard_map(
        shards,
        mesh=mesh,
        in_specs=(P(("grad", "col"), None), P(("grad", "col"), None)),
        out_specs=(P(("grad", "col"), None), P("col", None)),
        check_vma=False,
    )
```

```python
import math

import jax
import jax.numpy as jnp
from jax import lax
from jax.sharding import PartitionSpec as P

FF = 53248
POWER = 2
HALVES = 2


def all_sum(value, axes):
    for axis in axes:
        size = lax.axis_size(axis)
        if size & (size - 1):
            value = lax.psum(value, axis)
            continue
        step = 1
        while step < size:
            value = value + lax.ppermute(value, axis, [(i, i ^ step) for i in range(size)])
            step *= 2
    return value


def grad_gather(value):
    size = lax.axis_size("grad")
    index = lax.axis_index("grad")
    received = [value] + [
        lax.ppermute(value, "grad", [(i, (i + s) % size) for i in range(size)])
        for s in range(1, size)
    ]
    ordered = jnp.roll(jnp.stack(received)[::-1], index + 1, axis=0)
    return ordered.reshape((size * value.shape[0],) + value.shape[1:])


def shift_gather(value):
    size = lax.axis_size("grad")
    received = [value] + [
        lax.ppermute(value, "grad", [(i, (i + s) % size) for i in range(size)])
        for s in range(1, size)
    ]
    return jnp.concatenate(received, axis=0)


def shift_scatter_sum(value):
    size = lax.axis_size("grad")
    pieces = value.reshape((size, value.shape[0] // size) + value.shape[1:])
    total = pieces[0]
    for s in range(1, size):
        outgoing = pieces[(size - s) % size]
        total = total + lax.ppermute(outgoing, "grad", [(i, (i + s) % size) for i in range(size)])
    return total


def orthonormal(rows):
    partial_gram = lax.dot_general(
        rows,
        rows,
        (((0,), (0,)), ((), ())),
        precision=lax.Precision.HIGHEST,
        preferred_element_type=jnp.float32,
    )
    gram = all_sum(partial_gram, ("col", "grad"))
    lower_factor = jnp.linalg.cholesky(gram)
    identity = jnp.eye(gram.shape[0], dtype=gram.dtype)
    inverse = lax.linalg.triangular_solve(lower_factor, identity, left_side=True, lower=True)
    return lax.dot_general(
        rows,
        inverse,
        (((1,), (1,)), ((), ())),
        precision=lax.Precision.HIGHEST,
        preferred_element_type=jnp.float32,
    )


def shards(gradient, test_matrix):
    n_grad = lax.axis_size("grad")
    n_col = lax.axis_size("col")
    n_rows, n_ff = gradient.shape
    piece = n_ff // (n_col * n_grad)
    half = piece // HALVES
    test_rows, gradient = lax.optimization_barrier((shift_gather(test_matrix), gradient))
    index = lax.axis_index("grad")
    split = gradient.reshape(n_rows, n_col, n_grad, HALVES, half)
    chunks = []
    for h in range(HALVES):
        part = split[:, :, :, h]
        received = [lax.dynamic_index_in_dim(part, index, axis=2, keepdims=False)]
        for s in range(1, n_grad):
            outgoing = lax.dynamic_index_in_dim(part, (index + s) % n_grad, axis=2, keepdims=False)
            received.append(
                lax.ppermute(outgoing, "grad", [(i, (i + s) % n_grad) for i in range(n_grad)])
            )
        moved = jnp.concatenate(received, axis=0)
        chunks.append(moved.reshape(n_grad * n_rows, n_col * half))

    def sketch_of(rows):
        parts = []
        for chunk in chunks:
            partial = lax.dot_general(
                chunk, rows, (((0,), (0,)), ((), ())), preferred_element_type=jnp.float32
            )
            parts.append(lax.psum_scatter(partial, "col", scatter_dimension=0, tiled=True))
        return jnp.concatenate(parts, axis=0)

    sketch = sketch_of(test_rows)
    for iteration in range(POWER + 1):
        basis_rows = orthonormal(sketch)
        basis_bf = lax.all_gather(
            basis_rows.astype(jnp.bfloat16).reshape(HALVES, half, -1), "col", axis=1, tiled=True
        )
        partial = jnp.dot(chunks[0], basis_bf[0], preferred_element_type=jnp.float32)
        for h in range(1, HALVES):
            partial = partial + jnp.dot(chunks[h], basis_bf[h], preferred_element_type=jnp.float32)
        reduced = shift_scatter_sum(partial)
        if iteration < POWER:
            sketch = sketch_of(shift_gather(reduced.astype(jnp.bfloat16)))
    projector = grad_gather(basis_rows * math.sqrt(FF))
    return (reduced, projector)


def solution(mesh):
    return jax.shard_map(
        shards,
        mesh=mesh,
        in_specs=(P(("grad", "col"), None), P(("grad", "col"), None)),
        out_specs=(P(("grad", "col"), None), P("col", None)),
        check_vma=False,
    )
```
